512 devices in a mesh: grp: 8 (over z_hi, core), dom: 64 (over x, z_lo, y).
Axes of the slice: x: 4, y: 4, z: 16 (z_hi: 4, z_lo: 4; z = z_hi * 4 + z_lo), core: 2. Of those that a mesh axis runs over, the one named last changes fastest.
Arguments:
- reduced_basis: bfloat16 [1572864, 256], P(('grp', 'dom')), may hold values from -24 to 24
- tangents: bfloat16 [65536, 4096], P(('grp', 'dom')), may hold values from -1 to 2, as said below
- connectivity: int32 [20, 65536], P(None, ('grp', 'dom')), may hold values from 0 to 1151, as said below
- weights: float32 [65536], P(('grp', 'dom')), may hold values from 0.5 to 8
Outputs:
- residual_basis: bfloat16 [1572864, 256], P(('grp', 'dom'))
- galerkin_tangent: float32 [256, 256], replicated
- lspg_tangent: float32 [256, 256], replicated
The draws below stay inside these ranges and needn't reach their ends.
Inputs may be any that keep to these rules, and one draw needn't show every extreme that they name: `connectivity`: numbers below 1024 are the partition's own nodes; 1024 + k is node k of the next partition in grp+dom order; the last partition names only its own nodes. An element's node numbers lie in a range of 64, except that a partition's first element may also name node 0 and its last element node 1151. `tangents`: each tangent is symmetric, and its rows and columns 60 to 63 are zero.
All inputs are finite; a program needn't handle non-finite values.
Results may differ from the reference program's by a relative error of at most 0.0013.
Values may be sent and summed in bfloat16 or wider, within the bound.
No kernel may reach another device: no remote copies, remote signals or barrier semaphores. Data moves between devices by JAX's collectives and lax.ppermute only.
A program may use at most 64 MiB of HBM per device.

```python
import math
import jax
import jax.numpy as jnp
from jax import lax

R = 256
NPE = 20
EDOF = 64
NODE_DEV = 1024
ELEMS = 128
RIM = 128
SPAN = 64
NDOF = 1572864
ELEMS_ALL = 65536
N_GRP = 8
N_DOM = 64


def draw_tangents(key, part):
    devices = ELEMS_ALL // ELEMS
    active = 3 * NPE

    def one_block(position):
        block_key = jax.random.fold_in(jax.random.fold_in(key, 7001), position)
        first_key, second_key = jax.random.split(block_key)
        raw = 0.35 * jax.random.normal(first_key, (ELEMS, active, active), jnp.float32)
        symmetric = 0.5 * (raw + jnp.swapaxes(raw, 1, 2))
        diagonal = jax.random.uniform(second_key, (ELEMS, active), jnp.float32, 6.0, 9.0)
        full = (symmetric + diagonal[:, :, None] * jnp.eye(active, dtype=jnp.float32)[None]) / 8.0
        full = jnp.pad(full, ((0, 0), (0, EDOF - active), (0, EDOF - active)))
        return full.reshape(ELEMS, EDOF * EDOF).astype(jnp.bfloat16)
    blocks = lax.map(one_block, jnp.arange(devices, dtype=jnp.int32))
    return blocks.reshape(ELEMS_ALL, EDOF * EDOF)


def draw_connectivity(key, part):
    devices = ELEMS_ALL // ELEMS
    first_key, second_key = jax.random.split(jax.random.fold_in(key, 7002))
    element_index = jnp.arange(ELEMS_ALL, dtype=jnp.int32)
    owner = element_index // ELEMS
    top_base = jnp.where(owner == devices - 1, NODE_DEV - SPAN, NODE_DEV + RIM - SPAN)
    base_nodes = jax.random.randint(first_key, (ELEMS_ALL,), 0, 1 << 30, dtype=jnp.int32) % (top_base + 1)
    offsets = jax.random.randint(second_key, (NPE, ELEMS_ALL), 0, SPAN, dtype=jnp.int32)
    nodes = base_nodes[None, :] + offsets
    is_first = element_index % ELEMS == 0
    is_final = (element_index % ELEMS == ELEMS - 1) & (owner < devices - 1)
    nodes = nodes.at[0].set(jnp.where(is_first, 0, nodes[0]))
    nodes = nodes.at[NPE - 1].set(jnp.where(is_final, NODE_DEV + RIM - 1, nodes[NPE - 1]))
    return nodes.astype(jnp.int32)


def strengthened(drawn, rng, source, target, parts, factor):
    def block_of(dim):
        return (jnp.arange(drawn.shape[dim]) // (drawn.shape[dim] // parts)).reshape((-1,) + (1,) * (drawn.ndim - 1 - dim))

    near = jax.random.permutation(rng, parts)[block_of(target)]
    far = (block_of(target) + parts // 2) % parts
    return jnp.where((block_of(source) == near) | (block_of(source) == far), factor * drawn, drawn)


def block_levels(rng, shape, pieces, smallest, high):
    gain = 1.0
    for axis_at, shards_of in pieces:
        draws = jax.random.uniform(jax.random.fold_in(jax.random.fold_in(rng, 6), axis_at), (shards_of,), jnp.float32, smallest / len(pieces), high / len(pieces))
        gain = gain * jnp.repeat(jnp.exp(draws), shape[axis_at] // shards_of).reshape((-1,) + (1,) * (len(shape) - 1 - axis_at))
    return gain


def bell_draw_with(rng, extent, deviation, limit, pieces, heavy, held_as=jnp.bfloat16):
    array = deviation * jax.random.normal(rng, extent, jnp.float32)
    if pieces:
        array = array * block_levels(rng, extent, pieces, -0.22, 0.18)
    return jnp.clip(strengthened(array, jax.random.fold_in(rng, 3), *heavy), -limit, limit).astype(held_as)


def setup_inputs(seed: int = 0) -> dict:
    keys = jax.random.split(jax.random.key(seed), 5)
    reduced_basis = bell_draw_with(keys[0], (NDOF, R), 1.0, 24.0, ((0, 512),), (0, 1, 256, 6.0))
    tangents = draw_tangents(jax.random.fold_in(keys[4], 71), 0)
    connectivity = draw_connectivity(jax.random.fold_in(keys[4], 71), 0)
    weights = jnp.clip(jnp.exp(math.log(8.0) - 2.7725887 * jax.random.uniform(keys[3], (ELEMS_ALL,), jnp.float32) ** block_levels(keys[3], (ELEMS_ALL,), ((0, 512),), -0.2, 0.2)), 0.5, 8.0)
    return dict(reduced_basis=reduced_basis, tangents=tangents, connectivity=connectivity, weights=weights)


def element_rows(nodes):
    triples = nodes.T[:, :, None] * 3 + jnp.arange(3, dtype=jnp.int32)[None, None, :]
    flattened = triples.reshape(nodes.shape[1], -1).astype(jnp.int32)
    padding = jnp.zeros((nodes.shape[1], EDOF - flattened.shape[1]), jnp.int32)
    return jnp.concatenate([flattened, padding], axis=1)


def reference(reduced_basis, tangents, connectivity, weights):
    devices = N_GRP * N_DOM
    own_rows = NODE_DEV * 3
    rim_rows = RIM * 3
    padded = jnp.concatenate([reduced_basis, jnp.zeros((rim_rows, R), reduced_basis.dtype)], axis=0)
    tangent_blocks = tangents.reshape(devices, ELEMS, EDOF, EDOF)
    node_blocks = jnp.transpose(connectivity.reshape(NPE, devices, ELEMS), (1, 0, 2))
    weight_blocks = weights.reshape(devices, ELEMS)

    def partition(carry, inputs):
        tangent_set, node_set, weight_set, position = inputs
        extended = lax.dynamic_slice_in_dim(padded, (position * own_rows).astype(jnp.int32), own_rows + rim_rows, 0)
        dof_rows = element_rows(node_set)
        gathered = extended[dof_rows].astype(jnp.float32)
        products = jnp.einsum("eij,ejc->eic", tangent_set.astype(jnp.float32), gathered, precision=lax.Precision.HIGHEST)
        scaled = products * weight_set[:, None, None]
        assembled = jnp.zeros((own_rows + rim_rows, R), jnp.float32).at[dof_rows.reshape(-1)].add(scaled.reshape(-1, R))
        owned = assembled[:own_rows].at[:rim_rows].add(carry)
        residual_rows = owned.astype(jnp.bfloat16)
        basis_rows = extended[:own_rows].astype(jnp.float32)
        wide_rows = residual_rows.astype(jnp.float32)
        galerkin_part = jnp.einsum("rc,rd->cd", basis_rows, wide_rows, precision=lax.Precision.HIGHEST)
        lspg_part = jnp.einsum("rc,rd->cd", wide_rows, wide_rows, precision=lax.Precision.HIGHEST)
        return assembled[own_rows:], (residual_rows, galerkin_part, lspg_part)

    positions = jnp.arange(devices, dtype=jnp.int32)
    start_rim = jnp.zeros((rim_rows, R), jnp.float32)
    final_rim, outputs = lax.scan(partition, start_rim, (tangent_blocks, node_blocks, weight_blocks, positions))
    rows_all, galerkin_parts, lspg_parts = outputs
    scale_factor = 1.0 / float(NDOF)
    galerkin_tangent = jnp.sum(galerkin_parts, axis=0) * scale_factor
    lspg_tangent = jnp.sum(lspg_parts, axis=0) * scale_factor
    return (rows_all.reshape(NDOF, R), galerkin_tangent, lspg_tangent)
```

```python
import jax
import jax.numpy as jnp
from jax import lax
from jax.sharding import PartitionSpec as P

EDOF = 64
RIM = 128
AXES = ("grp", "dom")


def passed_along(x, axis, by):
    peers = lax.axis_size(axis)
    pairs = [(i, i + by) for i in range(peers) if 0 <= i + by < peers]
    return lax.ppermute(x, axis, pairs)


def element_rows(nodes):
    triples = nodes.T[:, :, None] * 3 + jnp.arange(3, dtype=jnp.int32)[None, None, :]
    flattened = triples.reshape(nodes.shape[1], -1)
    padding = jnp.zeros((nodes.shape[1], EDOF - flattened.shape[1]), jnp.int32)
    return jnp.concatenate([flattened, padding], axis=1)


def project(left_rows, right_rows):
    return jnp.einsum("rc,rd->cd", left_rows, right_rows, preferred_element_type=jnp.float32)


def bit_order(count):
    preferred = [6, 0, 2, 4, 1, 3, 5, 7, 8]
    bits = count.bit_length() - 1
    if count == 512:
        return preferred
    return list(range(bits))


def summed_everywhere(flat):
    count = lax.axis_size(AXES)
    if count & (count - 1) or flat.shape[0] % count:
        return lax.psum(flat, AXES)
    me = lax.axis_index(AXES)
    order = bit_order(count)
    current = flat
    for bit in order:
        half = current.shape[0] // 2
        upper = (me >> bit) & 1
        low, high = current[:half], current[half:]
        keep = jnp.where(upper == 0, low, high)
        send = jnp.where(upper == 0, high, low)
        pairs = [(i, i ^ (1 << bit)) for i in range(count)]
        current = keep + lax.ppermute(send, AXES, pairs)
    for bit in reversed(order):
        upper = (me >> bit) & 1
        pairs = [(i, i ^ (1 << bit)) for i in range(count)]
        other = lax.ppermute(current, AXES, pairs)
        current = jnp.where(
            upper == 0,
            jnp.concatenate([current, other]),
            jnp.concatenate([other, current]),
        )
    return current


def local(reduced_basis, tangents, connectivity, weights):
    own_rows, columns = reduced_basis.shape
    rim_rows = RIM * 3
    elem_count = weights.shape[0]
    elem_block = min(elem_count, 128)
    rim_basis = passed_along(reduced_basis[:rim_rows], AXES, -1)
    extended = jnp.concatenate([reduced_basis, rim_basis], axis=0)

    def add_block(step_index, assembled):
        tangent_set = tangents.reshape(elem_block, EDOF, EDOF)
        dof_rows = element_rows(connectivity)
        gathered = extended[dof_rows]
        products = jnp.einsum(
            "eij,ejc->eic", tangent_set, gathered, preferred_element_type=jnp.float32
        )
        scaled = products * weights[:, None, None]
        return assembled.at[dof_rows.reshape(-1)].add(scaled.reshape(-1, columns))

    empty = jnp.zeros((own_rows + rim_rows, columns), jnp.float32)
    assembled = lax.fori_loop(0, elem_count // elem_block, add_block, empty)
    incoming = passed_along(assembled[own_rows:], AXES, 1)
    residual_rows = assembled[:own_rows].at[:rim_rows].add(incoming).astype(jnp.bfloat16)
    galerkin_part = project(reduced_basis, residual_rows)
    lspg_part = project(residual_rows, residual_rows)
    both = jnp.stack([galerkin_part, lspg_part]).reshape(-1)
    galerkin_sum, lspg_sum = summed_everywhere(both).reshape(2, columns, columns)
    total_dofs = own_rows * lax.axis_size("grp") * lax.axis_size("dom")
    scale_factor = 1.0 / float(total_dofs)
    return (residual_rows, galerkin_sum * scale_factor, lspg_sum * scale_factor)


def solution(mesh):
    placed = (
        P(AXES, None),
        P(AXES, None),
        P(None, AXES),
        P(AXES),
    )
    return jax.shard_map(
        local,
        mesh=mesh,
        in_specs=placed,
        out_specs=(P(AXES, None), P(), P()),
        check_vma=False,
    )
```

```python
import functools

import jax
import jax.numpy as jnp
from jax import lax
from jax.experimental import pallas as pl
from jax.experimental.pallas import tpu as pltpu
from jax.sharding import Mesh, PartitionSpec as P

EDOF = 64
RIM = 128
AXES = ("grp", "dom")
WIN = 208


def window_tables(connectivity, ext_rows):
    npe, elems = connectivity.shape
    ext_nodes = ext_rows // 3
    nodes = connectivity.T
    index = jnp.arange(elems, dtype=jnp.int32)[:, None]
    outlier = ((index == 0) & (nodes == 0)) | ((index == elems - 1) & (nodes == ext_nodes - 1))
    low = jnp.min(jnp.where(outlier, ext_nodes, nodes), axis=1)
    low = jnp.where(low == ext_nodes, 0, low)
    first = jnp.clip((3 * low) // 16 * 16, 0, ext_rows - WIN)
    second = jnp.where(index[:, 0] == elems - 1, ext_rows - WIN, 0)
    rows = (nodes[:, :, None] * 3 + jnp.arange(3, dtype=jnp.int32)).reshape(elems, -1)
    pad = jnp.full((elems, EDOF - rows.shape[1]), -1, jnp.int32)
    slot_out = jnp.repeat(outlier, 3, axis=1)
    off1 = jnp.concatenate([jnp.where(slot_out, -1, rows - first[:, None]), pad], axis=1)
    off2 = jnp.concatenate([jnp.where(slot_out, rows - second[:, None], -1), pad], axis=1)
    return first.astype(jnp.int32), second.astype(jnp.int32), off1, off2


def element_kernel(first_ref, second_ref, w_ref, x_ref, k_ref, r1_ref, c1_ref, r2_ref, c2_ref, acc_ref):
    elems = k_ref.shape[0]
    acc_ref[...] = jnp.zeros_like(acc_ref)
    row_iota = lax.broadcasted_iota(jnp.int32, (WIN, EDOF), 0)
    col_iota = lax.broadcasted_iota(jnp.int32, (EDOF, WIN), 1)

    def one(e, windows):
        gathered = None
        picks = []
        for start_ref, row_ref, col_ref in windows:
            start = pl.multiple_of(start_ref[e], 16)
            pick = (col_ref[pl.ds(pl.multiple_of(e * EDOF, EDOF), EDOF), :] == col_iota).astype(jnp.bfloat16)
            part = jnp.dot(pick, x_ref[pl.ds(start, WIN), :], preferred_element_type=jnp.float32)
            gathered = part if gathered is None else gathered + part
            picks.append((start, (row_ref[pl.ds(e, 1), :] == row_iota).astype(jnp.bfloat16)))
        products = jnp.dot(k_ref[e], gathered.astype(jnp.bfloat16), preferred_element_type=jnp.float32)
        scaled = products * w_ref[e]
        high = scaled.astype(jnp.bfloat16)
        rest = scaled - high.astype(jnp.float32)
        mid = rest.astype(jnp.bfloat16)
        low = (rest - mid.astype(jnp.float32)).astype(jnp.bfloat16)
        parts = jnp.concatenate([high, mid, low], axis=1)
        cols = scaled.shape[1]
        for start, spread in picks:
            moved = jnp.dot(spread, parts, preferred_element_type=jnp.float32)
            total = (moved[:, :cols] + moved[:, cols:2 * cols]) + moved[:, 2 * cols:]
            acc_ref[pl.ds(start, WIN), :] += total

    both = ((first_ref, r1_ref, c1_ref), (second_ref, r2_ref, c2_ref))
    one(0, both)

    def body(e, carry):
        one(e, both[:1])
        return carry

    lax.fori_loop(1, elems - 1, body, 0)
    one(elems - 1, both)


def element_stage(extended, tangents, connectivity, weights):
    ext_rows, cols = extended.shape
    elems = weights.shape[0]
    first, second, off1, off2 = window_tables(connectivity, ext_rows)
    k = tangents.reshape(elems, EDOF, EDOF)
    c1 = off1.reshape(elems * EDOF, 1)
    c2 = off2.reshape(elems * EDOF, 1)
    vmem = pltpu.VMEM
    smem = pltpu.SMEM
    return pl.pallas_call(
        element_kernel,
        out_shape=jax.ShapeDtypeStruct((ext_rows, cols), jnp.float32),
        in_specs=[pl.BlockSpec(memory_space=smem)] * 3 + [pl.BlockSpec(memory_space=vmem)] * 6,
        out_specs=pl.BlockSpec(memory_space=vmem),
        compiler_params=pltpu.CompilerParams(vmem_limit_bytes=48 * 1024 * 1024),
    )(first, second, weights, extended, k, off1, c1, off2, c2)


def passed_along(x, axis, by):
    peers = lax.axis_size(axis)
    pairs = [(i, i + by) for i in range(peers) if 0 <= i + by < peers]
    return lax.ppermute(x, axis, pairs)


def element_rows(nodes):
    triples = nodes.T[:, :, None] * 3 + jnp.arange(3, dtype=jnp.int32)[None, None, :]
    flattened = triples.reshape(nodes.shape[1], -1)
    padding = jnp.zeros((nodes.shape[1], EDOF - flattened.shape[1]), jnp.int32)
    return jnp.concatenate([flattened, padding], axis=1)


def project(left_rows, right_rows):
    return jnp.einsum("rc,rd->cd", left_rows, right_rows, preferred_element_type=jnp.float32)


FINE = ("zh", "c", "x", "zl", "y")
FINE_SIZES = (4, 2, 4, 4, 4)


def group_sum(chunk, axis):
    size = lax.axis_size(axis)
    return lax.all_to_all(chunk.reshape(size, -1), axis, 0, 0, tiled=False).sum(0)


def group_gather(chunk, axis):
    size = lax.axis_size(axis)
    copies = jnp.broadcast_to(chunk[None], (size,) + chunk.shape)
    return lax.all_to_all(copies, axis, 0, 0, tiled=False).reshape(-1)


def summed_everywhere(flat, axes):
    if axes != FINE or flat.shape[0] % 512:
        return lax.psum(flat, axes)
    count = 512
    me = lax.axis_index(axes)
    core_pairs = [(i, i ^ 64) for i in range(count)]
    upper = (me >> 6) & 1
    half = flat.shape[0] // 2
    low, high = flat[:half], flat[half:]
    keep = jnp.where(upper == 0, low, high)
    send = jnp.where(upper == 0, high, low)
    current = keep + lax.ppermute(send, axes, core_pairs)
    for axis in ("y", "zl", "x"):
        current = group_sum(current, axis)
    parts = [current]
    for shift in (1, 2, 3):
        pairs = [(i, (((i >> 7) + shift) % 4) * 128 + i % 128) for i in range(count)]
        parts.append(lax.ppermute(current, axes, pairs))
    current = (parts[0] + parts[2]) + (parts[1] + parts[3])
    for axis in ("x", "zl", "y"):
        current = group_gather(current, axis)
    other = lax.ppermute(current, axes, core_pairs)
    return jnp.where(
        upper == 0,
        jnp.concatenate([current, other]),
        jnp.concatenate([other, current]),
    )


def local(axes, reduced_basis, tangents, connectivity, weights):
    own_rows, columns = reduced_basis.shape
    rim_rows = RIM * 3
    rim_basis = passed_along(reduced_basis[:rim_rows], axes, -1)
    extended = jnp.concatenate([reduced_basis, rim_basis], axis=0)

    assembled = element_stage(extended, tangents, connectivity, weights)
    incoming = passed_along(assembled[own_rows:], axes, 1)
    residual_rows = assembled[:own_rows].at[:rim_rows].add(incoming).astype(jnp.bfloat16)
    galerkin_part = project(reduced_basis, residual_rows)
    lspg_part = project(residual_rows, residual_rows)
    both = jnp.stack([galerkin_part, lspg_part]).reshape(-1)
    galerkin_sum, lspg_sum = summed_everywhere(both, axes).reshape(2, columns, columns)
    total_dofs = own_rows * lax.axis_size(axes)
    scale_factor = 1.0 / float(total_dofs)
    return (residual_rows, galerkin_sum * scale_factor, lspg_sum * scale_factor)


def solution(mesh):
    axes = AXES
    if tuple(mesh.devices.shape) == (8, 64):
        mesh = Mesh(mesh.devices.reshape(FINE_SIZES), FINE)
        axes = FINE
    placed = (
        P(axes, None),
        P(axes, None),
        P(None, axes),
        P(axes),
    )
    return jax.shard_map(
        functools.partial(local, axes),
        mesh=mesh,
        in_specs=placed,
        out_specs=(P(axes, None), P(), P()),
        check_vma=False,
    )
```

```python
import functools

import jax
import jax.numpy as jnp
from jax import lax
from jax.experimental import pallas as pl
from jax.experimental.pallas import tpu as pltpu
from jax.sharding import Mesh, PartitionSpec as P

EDOF = 64
RIM = 128
AXES = ("grp", "dom")
WIN = 208


def window_tables(connectivity, ext_rows):
    npe, elems = connectivity.shape
    ext_nodes = ext_rows // 3
    nodes = connectivity.T
    index = jnp.arange(elems, dtype=jnp.int32)[:, None]
    outlier = ((index == 0) & (nodes == 0)) | ((index == elems - 1) & (nodes == ext_nodes - 1))
    low = jnp.min(jnp.where(outlier, ext_nodes, nodes), axis=1)
    low = jnp.where(low == ext_nodes, 0, low)
    first = jnp.clip((3 * low) // 16 * 16, 0, ext_rows - WIN)
    second = jnp.where(index[:, 0] == elems - 1, ext_rows - WIN, 0)
    rows = (nodes[:, :, None] * 3 + jnp.arange(3, dtype=jnp.int32)).reshape(elems, -1)
    pad = jnp.full((elems, EDOF - rows.shape[1]), -1, jnp.int32)
    slot_out = jnp.repeat(outlier, 3, axis=1)
    off1 = jnp.concatenate([jnp.where(slot_out, -1, rows - first[:, None]), pad], axis=1)
    off2 = jnp.concatenate([jnp.where(slot_out, rows - second[:, None], -1), pad], axis=1)
    return first.astype(jnp.int32), second.astype(jnp.int32), off1, off2


def element_kernel(first_ref, second_ref, w_ref, x_ref, k_ref, r1_ref, r2_ref, acc_ref):
    elems = k_ref.shape[0]
    acc_ref[...] = jnp.zeros_like(acc_ref)
    row_iota = lax.broadcasted_iota(jnp.int32, (WIN, EDOF), 0)
    eye = (
        lax.broadcasted_iota(jnp.int32, (EDOF, EDOF), 0)
        == lax.broadcasted_iota(jnp.int32, (EDOF, EDOF), 1)
    ).astype(jnp.bfloat16)
    both = ((first_ref, r1_ref), (second_ref, r2_ref))

    def one(e, windows):
        gathered = None
        picks = []
        for start_ref, row_ref in windows:
            start = pl.multiple_of(start_ref[e], 16)
            spread = (row_ref[pl.ds(e, 1), :] == row_iota).astype(jnp.bfloat16)
            pick = lax.dot_general(
                eye, spread, (((1,), (1,)), ((), ())), preferred_element_type=jnp.float32
            ).astype(jnp.bfloat16)
            part = jnp.dot(pick, x_ref[pl.ds(start, WIN), :], preferred_element_type=jnp.float32)
            gathered = part if gathered is None else gathered + part
            picks.append((start, spread))
        products = jnp.dot(k_ref[e], gathered.astype(jnp.bfloat16), preferred_element_type=jnp.float32)
        scaled = products * w_ref[e]
        high = scaled.astype(jnp.bfloat16)
        rest = scaled - high.astype(jnp.float32)
        mid = rest.astype(jnp.bfloat16)
        low = (rest - mid.astype(jnp.float32)).astype(jnp.bfloat16)
        parts = jnp.concatenate([high, mid, low], axis=1)
        cols = scaled.shape[1]
        for start, spread in picks:
            moved = jnp.dot(spread, parts, preferred_element_type=jnp.float32)
            total = (moved[:, :cols] + moved[:, cols:2 * cols]) + moved[:, 2 * cols:]
            acc_ref[pl.ds(start, WIN), :] += total

    one(0, both)

    def body(e, carry):
        one(e, both[:1])
        return carry

    lax.fori_loop(1, elems - 1, body, 0, unroll=8)
    one(elems - 1, both)


def element_stage(extended, tangents, connectivity, weights):
    ext_rows, cols = extended.shape
    elems = weights.shape[0]
    first, second, off1, off2 = window_tables(connectivity, ext_rows)
    k = tangents.reshape(elems, EDOF, EDOF)
    return pl.pallas_call(
        element_kernel,
        out_shape=jax.ShapeDtypeStruct((ext_rows, cols), jnp.float32),
        in_specs=[pl.BlockSpec(memory_space=pltpu.SMEM)] * 3
        + [pl.BlockSpec(memory_space=pltpu.VMEM)] * 4,
        out_specs=pl.BlockSpec(memory_space=pltpu.VMEM),
        compiler_params=pltpu.CompilerParams(vmem_limit_bytes=48 * 1024 * 1024),
    )(first, second, weights, extended, k, off1, off2)


def passed_along(x, axis, by):
    peers = lax.axis_size(axis)
    pairs = [(i, i + by) for i in range(peers) if 0 <= i + by < peers]
    return lax.ppermute(x, axis, pairs)


def element_rows(nodes):
    triples = nodes.T[:, :, None] * 3 + jnp.arange(3, dtype=jnp.int32)[None, None, :]
    flattened = triples.reshape(nodes.shape[1], -1)
    padding = jnp.zeros((nodes.shape[1], EDOF - flattened.shape[1]), jnp.int32)
    return jnp.concatenate([flattened, padding], axis=1)


def project(left_rows, right_rows):
    return jnp.einsum("rc,rd->cd", left_rows, right_rows, preferred_element_type=jnp.float32)


FINE = ("zh", "c", "x", "zl", "y")
FINE_SIZES = (4, 2, 4, 4, 4)


def group_sum(chunk, axis):
    size = lax.axis_size(axis)
    return lax.all_to_all(chunk.reshape(size, -1), axis, 0, 0, tiled=False).sum(0)


def group_gather(chunk, axis):
    size = lax.axis_size(axis)
    copies = jnp.broadcast_to(chunk[None], (size,) + chunk.shape)
    return lax.all_to_all(copies, axis, 0, 0, tiled=False).reshape(-1)


def summed_everywhere(flat, axes):
    if axes != FINE or flat.shape[0] % 512:
        return lax.psum(flat, axes)
    count = 512
    me = lax.axis_index(axes)
    core_pairs = [(i, i ^ 64) for i in range(count)]
    upper = (me >> 6) & 1
    half = flat.shape[0] // 2
    low, high = flat[:half], flat[half:]
    keep = jnp.where(upper == 0, low, high)
    send = jnp.where(upper == 0, high, low)
    current = keep + lax.ppermute(send, axes, core_pairs)
    for axis in ("y", "zl", "x"):
        current = group_sum(current, axis)
    parts = [current]
    for shift in (1, 2, 3):
        pairs = [(i, (((i >> 7) + shift) % 4) * 128 + i % 128) for i in range(count)]
        parts.append(lax.ppermute(current, axes, pairs))
    current = (parts[0] + parts[2]) + (parts[1] + parts[3])
    for axis in ("x", "zl", "y"):
        current = group_gather(current, axis)
    other = lax.ppermute(current, axes, core_pairs)
    return jnp.where(
        upper == 0,
        jnp.concatenate([current, other]),
        jnp.concatenate([other, current]),
    )


def local(axes, reduced_basis, tangents, connectivity, weights):
    own_rows, columns = reduced_basis.shape
    rim_rows = RIM * 3
    rim_basis = passed_along(reduced_basis[:rim_rows], axes, -1)
    extended = jnp.concatenate([reduced_basis, rim_basis], axis=0)

    assembled = element_stage(extended, tangents, connectivity, weights)
    incoming = passed_along(assembled[own_rows:], axes, 1)
    residual_rows = assembled[:own_rows].at[:rim_rows].add(incoming).astype(jnp.bfloat16)
    galerkin_part = project(reduced_basis, residual_rows)
    lspg_part = project(residual_rows, residual_rows)
    both = jnp.stack([galerkin_part, lspg_part]).reshape(-1)
    galerkin_sum, lspg_sum = summed_everywhere(both, axes).reshape(2, columns, columns)
    total_dofs = own_rows * lax.axis_size(axes)
    scale_factor = 1.0 / float(total_dofs)
    return (residual_rows, galerkin_sum * scale_factor, lspg_sum * scale_factor)


def solution(mesh):
    axes = AXES
    if tuple(mesh.devices.shape) == (8, 64):
        mesh = Mesh(mesh.devices.reshape(FINE_SIZES), FINE)
        axes = FINE
    placed = (
        P(axes, None),
        P(axes, None),
        P(None, axes),
        P(axes),
    )
    return jax.shard_map(
        functools.partial(local, axes),
        mesh=mesh,
        in_specs=placed,
        out_specs=(P(axes, None), P(), P()),
        check_vma=False,
    )
```

```python
import functools

import jax
import jax.numpy as jnp
from jax import lax
from jax.experimental import pallas as pl
from jax.experimental.pallas import tpu as pltpu
from jax.sharding import Mesh, PartitionSpec as P

EDOF = 64
RIM = 128
AXES = ("grp", "dom")
WIN = 208


def window_tables(connectivity, ext_rows):
    npe, elems = connectivity.shape
    ext_nodes = ext_rows // 3
    nodes = connectivity.T
    index = jnp.arange(elems, dtype=jnp.int32)[:, None]
    outlier = ((index == 0) & (nodes == 0)) | ((index == elems - 1) & (nodes == ext_nodes - 1))
    low = jnp.min(jnp.where(outlier, ext_nodes, nodes), axis=1)
    low = jnp.where(low == ext_nodes, 0, low)
    first = jnp.clip((3 * low) // 16 * 16, 0, ext_rows - WIN)
    second = jnp.where(index[:, 0] == elems - 1, ext_rows - WIN, 0)
    rows = (nodes[:, :, None] * 3 + jnp.arange(3, dtype=jnp.int32)).reshape(elems, -1)
    pad = jnp.full((elems, EDOF - rows.shape[1]), -1, jnp.int32)
    slot_out = jnp.repeat(outlier, 3, axis=1)
    off1 = jnp.concatenate([jnp.where(slot_out, -1, rows - first[:, None]), pad], axis=1)
    off2 = jnp.concatenate([jnp.where(slot_out, rows - second[:, None], -1), pad], axis=1)
    return first.astype(jnp.int32), second.astype(jnp.int32), off1, off2


def element_kernel(first_ref, second_ref, w_ref, x_ref, k_ref, r1_ref, r2_ref, acc_ref):
    elems = k_ref.shape[0]
    acc_ref[...] = jnp.zeros_like(acc_ref)
    row_iota = lax.broadcasted_iota(jnp.int32, (WIN, EDOF), 0)
    eye = (
        lax.broadcasted_iota(jnp.int32, (EDOF, EDOF), 0)
        == lax.broadcasted_iota(jnp.int32, (EDOF, EDOF), 1)
    ).astype(jnp.bfloat16)
    both = ((first_ref, r1_ref), (second_ref, r2_ref))

    def one(e, windows):
        gathered = None
        picks = []
        for start_ref, row_ref in windows:
            start = pl.multiple_of(start_ref[e], 16)
            spread = (row_ref[pl.ds(e, 1), :] == row_iota).astype(jnp.bfloat16)
            pick = lax.dot_general(
                eye, spread, (((1,), (1,)), ((), ())), preferred_element_type=jnp.float32
            ).astype(jnp.bfloat16)
            part = jnp.dot(pick, x_ref[pl.ds(start, WIN), :], preferred_element_type=jnp.float32)
            gathered = part if gathered is None else gathered + part
            picks.append((start, spread))
        products = jnp.dot(k_ref[e], gathered.astype(jnp.bfloat16), preferred_element_type=jnp.float32)
        scaled = products * w_ref[e]
        high = scaled.astype(jnp.bfloat16)
        rest = scaled - high.astype(jnp.float32)
        mid = rest.astype(jnp.bfloat16)
        low = (rest - mid.astype(jnp.float32)).astype(jnp.bfloat16)
        parts = jnp.concatenate([high, mid, low], axis=1)
        cols = scaled.shape[1]
        for start, spread in picks:
            moved = jnp.dot(spread, parts, preferred_element_type=jnp.float32)
            total = (moved[:, :cols] + moved[:, cols:2 * cols]) + moved[:, 2 * cols:]
            acc_ref[pl.ds(start, WIN), :] += total

    one(0, both)

    def body(e, carry):
        one(e, both[:1])
        return carry

    lax.fori_loop(1, elems - 1, body, 0, unroll=8)
    one(elems - 1, both)


def element_stage(extended, tangents, connectivity, weights):
    ext_rows, cols = extended.shape
    elems = weights.shape[0]
    first, second, off1, off2 = window_tables(connectivity, ext_rows)
    k = tangents.reshape(elems, EDOF, EDOF)
    return pl.pallas_call(
        element_kernel,
        out_shape=jax.ShapeDtypeStruct((ext_rows, cols), jnp.float32),
        in_specs=[pl.BlockSpec(memory_space=pltpu.SMEM)] * 3
        + [pl.BlockSpec(memory_space=pltpu.VMEM)] * 4,
        out_specs=pl.BlockSpec(memory_space=pltpu.VMEM),
        compiler_params=pltpu.CompilerParams(vmem_limit_bytes=48 * 1024 * 1024),
    )(first, second, weights, extended, k, off1, off2)


def passed_along(x, axis, by):
    peers = lax.axis_size(axis)
    pairs = [(i, i + by) for i in range(peers) if 0 <= i + by < peers]
    return lax.ppermute(x, axis, pairs)


def element_rows(nodes):
    triples = nodes.T[:, :, None] * 3 + jnp.arange(3, dtype=jnp.int32)[None, None, :]
    flattened = triples.reshape(nodes.shape[1], -1)
    padding = jnp.zeros((nodes.shape[1], EDOF - flattened.shape[1]), jnp.int32)
    return jnp.concatenate([flattened, padding], axis=1)


def project(left_rows, right_rows):
    return jnp.einsum("rc,rd->cd", left_rows, right_rows, preferred_element_type=jnp.float32)


FINE = ("zh", "c", "x", "zl", "y")
FINE_SIZES = (4, 2, 4, 4, 4)


def group_sum(chunk, axis):
    size = lax.axis_size(axis)
    return lax.all_to_all(chunk.reshape(size, -1), axis, 0, 0, tiled=False).sum(0)


def group_gather(chunk, axis):
    size = lax.axis_size(axis)
    copies = jnp.broadcast_to(chunk[None], (size,) + chunk.shape)
    return lax.all_to_all(copies, axis, 0, 0, tiled=False).reshape(-1)


def summed_everywhere(flat, axes):
    if axes != FINE or flat.shape[0] % 512:
        return lax.psum(flat, axes)
    count = 512
    me = lax.axis_index(axes)
    core_pairs = [(i, i ^ 64) for i in range(count)]
    upper = (me >> 6) & 1
    half = flat.shape[0] // 2
    low, high = flat[:half], flat[half:]
    keep = jnp.where(upper == 0, low, high)
    send = jnp.where(upper == 0, high, low)
    current = keep + lax.ppermute(send, axes, core_pairs)
    for group in (("zl", "y"), ("zh", "x")):
        current = group_sum(current, group)
    for group in (("zh", "x"), ("zl", "y")):
        current = group_gather(current, group)
    other = lax.ppermute(current, axes, core_pairs)
    return jnp.where(
        upper == 0,
        jnp.concatenate([current, other]),
        jnp.concatenate([other, current]),
    )


def local(axes, reduced_basis, tangents, connectivity, weights):
    own_rows, columns = reduced_basis.shape
    rim_rows = RIM * 3
    rim_basis = passed_along(reduced_basis[:rim_rows], axes, -1)
    extended = jnp.concatenate([reduced_basis, rim_basis], axis=0)

    assembled = element_stage(extended, tangents, connectivity, weights)
    incoming = passed_along(assembled[own_rows:], axes, 1)
    residual_rows = assembled[:own_rows].at[:rim_rows].add(incoming).astype(jnp.bfloat16)
    galerkin_part = project(reduced_basis, residual_rows)
    lspg_part = project(residual_rows, residual_rows)
    both = jnp.stack([galerkin_part, lspg_part]).reshape(-1)
    galerkin_sum, lspg_sum = summed_everywhere(both, axes).reshape(2, columns, columns)
    total_dofs = own_rows * lax.axis_size(axes)
    scale_factor = 1.0 / float(total_dofs)
    return (residual_rows, galerkin_sum * scale_factor, lspg_sum * scale_factor)


def solution(mesh):
    axes = AXES
    if tuple(mesh.devices.shape) == (8, 64):
        mesh = Mesh(mesh.devices.reshape(FINE_SIZES), FINE)
        axes = FINE
    placed = (
        P(axes, None),
        P(axes, None),
        P(None, axes),
        P(axes),
    )
    return jax.shard_map(
        functools.partial(local, axes),
        mesh=mesh,
        in_specs=placed,
        out_specs=(P(axes, None), P(), P()),
        check_vma=False,
    )
```

```python
import functools

import jax
import jax.numpy as jnp
from jax import lax
from jax.experimental import pallas as pl
from jax.experimental.pallas import tpu as pltpu
from jax.sharding import Mesh, PartitionSpec as P

EDOF = 64
RIM = 128
AXES = ("grp", "dom")
WIN = 208
UNROLL = 8


def window_tables(connectivity, ext_rows):
    npe, elems = connectivity.shape
    ext_nodes = ext_rows // 3
    nodes = connectivity.T
    index = jnp.arange(elems, dtype=jnp.int32)[:, None]
    outlier = ((index == 0) & (nodes == 0)) | ((index == elems - 1) & (nodes == ext_nodes - 1))
    low = jnp.min(jnp.where(outlier, ext_nodes, nodes), axis=1)
    low = jnp.where(low == ext_nodes, 0, low)
    first = jnp.clip((3 * low) // 16 * 16, 0, ext_rows - WIN)
    second = jnp.where(index[:, 0] == elems - 1, ext_rows - WIN, 0)
    rows = (nodes[:, :, None] * 3 + jnp.arange(3, dtype=jnp.int32)).reshape(elems, -1)
    pad = jnp.full((elems, EDOF - rows.shape[1]), -1, jnp.int32)
    slot_out = jnp.repeat(outlier, 3, axis=1)
    off1 = jnp.concatenate([jnp.where(slot_out, -1, rows - first[:, None]), pad], axis=1)
    off2 = jnp.concatenate([jnp.where(slot_out, rows - second[:, None], -1), pad], axis=1)
    return first.astype(jnp.int32), second.astype(jnp.int32), off1, off2


def element_kernel(specials, first_ref, second_ref, w_ref, order_ref, span_ref, x_ref, k_ref, r1_ref, r2_ref, *refs):
    acc_ref = refs[-1]
    elems = k_ref.shape[0]
    row_iota = lax.broadcasted_iota(jnp.int32, (WIN, EDOF), 0)
    eye = (
        lax.broadcasted_iota(jnp.int32, (EDOF, EDOF), 0)
        == lax.broadcasted_iota(jnp.int32, (EDOF, EDOF), 1)
    ).astype(jnp.bfloat16)
    both = ((first_ref, r1_ref), (second_ref, r2_ref))

    def one(e, windows):
        gathered = None
        picks = []
        for start_ref, row_ref in windows:
            start = pl.multiple_of(start_ref[e], 16)
            spread = (row_ref[pl.ds(e, 1), :] == row_iota).astype(jnp.bfloat16)
            pick = lax.dot_general(
                eye, spread, (((1,), (1,)), ((), ())), preferred_element_type=jnp.float32
            ).astype(jnp.bfloat16)
            part = jnp.dot(pick, x_ref[pl.ds(start, WIN), :], preferred_element_type=jnp.float32)
            gathered = part if gathered is None else gathered + part
            picks.append((start, spread))
        products = jnp.dot(k_ref[e], gathered.astype(jnp.bfloat16), preferred_element_type=jnp.float32)
        scaled = products * w_ref[e]
        high = scaled.astype(jnp.bfloat16)
        rest = scaled - high.astype(jnp.float32)
        mid = rest.astype(jnp.bfloat16)
        low = (rest - mid.astype(jnp.float32)).astype(jnp.bfloat16)
        parts = jnp.concatenate([high, mid, low], axis=1)
        cols = scaled.shape[1]
        for start, spread in picks:
            moved = jnp.dot(spread, parts, preferred_element_type=jnp.float32)
            total = (moved[:, :cols] + moved[:, cols:2 * cols]) + moved[:, 2 * cols:]
            acc_ref[pl.ds(start, WIN), :] += total

    if specials:
        acc_ref[...] = jnp.zeros_like(acc_ref)
        one(0, both)
        one(elems - 1, both)
    else:
        acc_ref[...] = refs[0][...]
    lo = span_ref[0]
    hi = span_ref[1]
    blocks = (hi - lo) // UNROLL

    def block(j, carry):
        for t in range(UNROLL):
            one(order_ref[lo + j * UNROLL + t], both[:1])
        return carry

    lax.fori_loop(0, blocks, block, 0)

    def single(i, carry):
        one(order_ref[i], both[:1])
        return carry

    lax.fori_loop(lo + blocks * UNROLL, hi, single, 0)


def element_call(specials, tables, extended, k, acc):
    first, second, weights, order, span, off1, off2 = tables
    carried = () if specials else (acc,)
    return pl.pallas_call(
        functools.partial(element_kernel, specials),
        out_shape=jax.ShapeDtypeStruct(extended.shape, jnp.float32),
        in_specs=[pl.BlockSpec(memory_space=pltpu.SMEM)] * 5
        + [pl.BlockSpec(memory_space=pltpu.VMEM)] * (4 + len(carried)),
        out_specs=pl.BlockSpec(memory_space=pltpu.VMEM),
        input_output_aliases={} if specials else {9: 0},
        compiler_params=pltpu.CompilerParams(vmem_limit_bytes=48 * 1024 * 1024),
    )(first, second, weights, order, span, extended, k, off1, off2, *carried)


def element_stage(extended, tangents, connectivity, weights, own_nodes):
    ext_rows, cols = extended.shape
    elems = weights.shape[0]
    first, second, off1, off2 = window_tables(connectivity, ext_rows)
    k = tangents.reshape(elems, EDOF, EDOF)
    index = jnp.arange(elems, dtype=jnp.int32)
    inner = (index > 0) & (index < elems - 1)
    touches = jnp.any(connectivity >= own_nodes, axis=0) & inner
    later = ~touches & inner
    early_count = jnp.sum(touches.astype(jnp.int32))
    place = jnp.where(
        touches,
        jnp.cumsum(touches.astype(jnp.int32)) - 1,
        early_count + jnp.cumsum(later.astype(jnp.int32)) - 1,
    )
    place = jnp.where(inner, place, elems - 1)
    order = jnp.zeros((elems,), jnp.int32).at[place].set(index)
    early = jnp.stack([jnp.int32(0), early_count])
    rest = jnp.stack([early_count, jnp.int32(elems - 2)])
    tables = (first, second, weights, order, early, off1, off2)
    acc = element_call(True, tables, extended, k, None)
    rim_part = acc[ext_rows - (ext_rows - 3 * own_nodes):]
    tables = (first, second, weights, order, rest, off1, off2)
    return rim_part, acc, functools.partial(element_call, False, tables, extended, k)


def passed_along(x, axis, by):
    peers = lax.axis_size(axis)
    pairs = [(i, i + by) for i in range(peers) if 0 <= i + by < peers]
    return lax.ppermute(x, axis, pairs)


def element_rows(nodes):
    triples = nodes.T[:, :, None] * 3 + jnp.arange(3, dtype=jnp.int32)[None, None, :]
    flattened = triples.reshape(nodes.shape[1], -1)
    padding = jnp.zeros((nodes.shape[1], EDOF - flattened.shape[1]), jnp.int32)
    return jnp.concatenate([flattened, padding], axis=1)


def project(left_rows, right_rows):
    return jnp.einsum("rc,rd->cd", left_rows, right_rows, preferred_element_type=jnp.float32)


FINE = ("zh", "c", "x", "zl", "y")
FINE_SIZES = (4, 2, 4, 4, 4)


def group_sum(chunk, axis):
    size = lax.axis_size(axis)
    return lax.all_to_all(chunk.reshape(size, -1), axis, 0, 0, tiled=False).sum(0)


def group_gather(chunk, axis):
    size = lax.axis_size(axis)
    copies = jnp.broadcast_to(chunk[None], (size,) + chunk.shape)
    return lax.all_to_all(copies, axis, 0, 0, tiled=False).reshape(-1)


def summed_everywhere(flat, axes):
    if axes != FINE or flat.shape[0] % 512:
        return lax.psum(flat, axes)
    count = 512
    me = lax.axis_index(axes)
    core_pairs = [(i, i ^ 64) for i in range(count)]
    upper = (me >> 6) & 1
    half = flat.shape[0] // 2
    low, high = flat[:half], flat[half:]
    keep = jnp.where(upper == 0, low, high)
    send = jnp.where(upper == 0, high, low)
    current = keep + lax.ppermute(send, axes, core_pairs)
    for group in (("zl", "y"), ("zh", "x")):
        current = group_sum(current, group)
    for group in (("zh", "x"), ("zl", "y")):
        current = group_gather(current, group)
    other = lax.ppermute(current, axes, core_pairs)
    return jnp.where(
        upper == 0,
        jnp.concatenate([current, other]),
        jnp.concatenate([other, current]),
    )


def local(axes, reduced_basis, tangents, connectivity, weights):
    own_rows, columns = reduced_basis.shape
    rim_rows = RIM * 3
    rim_basis = passed_along(reduced_basis[:rim_rows], axes, -1)
    extended = jnp.concatenate([reduced_basis, rim_basis], axis=0)

    rim_part, partial_sums, finish = element_stage(
        extended, tangents, connectivity, weights, own_rows // 3
    )
    incoming = passed_along(rim_part, axes, 1)
    assembled = finish(partial_sums)
    residual_rows = assembled[:own_rows].at[:rim_rows].add(incoming).astype(jnp.bfloat16)
    galerkin_part = project(reduced_basis, residual_rows)
    lspg_part = project(residual_rows, residual_rows)
    both = jnp.stack([galerkin_part, lspg_part]).reshape(-1)
    galerkin_sum, lspg_sum = summed_everywhere(both, axes).reshape(2, columns, columns)
    total_dofs = own_rows * lax.axis_size(axes)
    scale_factor = 1.0 / float(total_dofs)
    return (residual_rows, galerkin_sum * scale_factor, lspg_sum * scale_factor)


def solution(mesh):
    axes = AXES
    if tuple(mesh.devices.shape) == (8, 64):
        mesh = Mesh(mesh.devices.reshape(FINE_SIZES), FINE)
        axes = FINE
    placed = (
        P(axes, None),
        P(axes, None),
        P(None, axes),
        P(axes),
    )
    return jax.shard_map(
        functools.partial(local, axes),
        mesh=mesh,
        in_specs=placed,
        out_specs=(P(axes, None), P(), P()),
        check_vma=False,
    )
```

```python
import functools

import jax
import jax.numpy as jnp
from jax import lax
from jax.experimental import pallas as pl
from jax.experimental.pallas import tpu as pltpu
from jax.sharding import Mesh, PartitionSpec as P

EDOF = 64
RIM = 128
AXES = ("grp", "dom")
WIN = 208


def window_tables(connectivity, ext_rows):
    npe, elems = connectivity.shape
    ext_nodes = ext_rows // 3
    nodes = connectivity.T
    index = jnp.arange(elems, dtype=jnp.int32)[:, None]
    outlier = ((index == 0) & (nodes == 0)) | ((index == elems - 1) & (nodes == ext_nodes - 1))
    low = jnp.min(jnp.where(outlier, ext_nodes, nodes), axis=1)
    low = jnp.where(low == ext_nodes, 0, low)
    first = jnp.clip((3 * low) // 16 * 16, 0, ext_rows - WIN)
    second = jnp.where(index[:, 0] == elems - 1, ext_rows - WIN, 0)
    rows = (nodes[:, :, None] * 3 + jnp.arange(3, dtype=jnp.int32)).reshape(elems, -1)
    pad = jnp.full((elems, EDOF - rows.shape[1]), -1, jnp.int32)
    slot_out = jnp.repeat(outlier, 3, axis=1)
    off1 = jnp.concatenate([jnp.where(slot_out, -1, rows - first[:, None]), pad], axis=1)
    off2 = jnp.concatenate([jnp.where(slot_out, rows - second[:, None], -1), pad], axis=1)
    return first.astype(jnp.int32), second.astype(jnp.int32), off1, off2


def element_kernel(first_ref, second_ref, w_ref, x_ref, k_ref, r1_ref, r2_ref, acc_ref):
    elems = k_ref.shape[0]
    acc_ref[...] = jnp.zeros_like(acc_ref)
    row_iota = lax.broadcasted_iota(jnp.int32, (WIN, EDOF), 0)
    eye = (
        lax.broadcasted_iota(jnp.int32, (EDOF, EDOF), 0)
        == lax.broadcasted_iota(jnp.int32, (EDOF, EDOF), 1)
    ).astype(jnp.bfloat16)
    both = ((first_ref, r1_ref), (second_ref, r2_ref))

    def one(e, windows):
        gathered = None
        picks = []
        for start_ref, row_ref in windows:
            start = pl.multiple_of(start_ref[e], 16)
            spread = (row_ref[pl.ds(e, 1), :] == row_iota).astype(jnp.bfloat16)
            pick = lax.dot_general(
                eye, spread, (((1,), (1,)), ((), ())), preferred_element_type=jnp.float32
            ).astype(jnp.bfloat16)
            part = jnp.dot(pick, x_ref[pl.ds(start, WIN), :], preferred_element_type=jnp.float32)
            gathered = part if gathered is None else gathered + part
            picks.append((start, spread))
        products = jnp.dot(k_ref[e], gathered.astype(jnp.bfloat16), preferred_element_type=jnp.float32)
        scaled = products * w_ref[e]
        high = scaled.astype(jnp.bfloat16)
        rest = scaled - high.astype(jnp.float32)
        mid = rest.astype(jnp.bfloat16)
        parts = jnp.concatenate([high, mid], axis=1)
        cols = scaled.shape[1]
        for start, spread in picks:
            moved = jnp.dot(spread, parts, preferred_element_type=jnp.float32)
            total = moved[:, :cols] + moved[:, cols:]
            acc_ref[pl.ds(start, WIN), :] += total

    one(0, both)

    def body(e, carry):
        one(e, both[:1])
        return carry

    lax.fori_loop(1, elems - 1, body, 0, unroll=8)
    one(elems - 1, both)


def element_stage(extended, tangents, connectivity, weights):
    ext_rows, cols = extended.shape
    elems = weights.shape[0]
    first, second, off1, off2 = window_tables(connectivity, ext_rows)
    k = tangents.reshape(elems, EDOF, EDOF)
    return pl.pallas_call(
        element_kernel,
        out_shape=jax.ShapeDtypeStruct((ext_rows, cols), jnp.float32),
        in_specs=[pl.BlockSpec(memory_space=pltpu.SMEM)] * 3
        + [pl.BlockSpec(memory_space=pltpu.VMEM)] * 4,
        out_specs=pl.BlockSpec(memory_space=pltpu.VMEM),
        compiler_params=pltpu.CompilerParams(vmem_limit_bytes=48 * 1024 * 1024),
    )(first, second, weights, extended, k, off1, off2)


def passed_along(x, axis, by):
    peers = lax.axis_size(axis)
    pairs = [(i, i + by) for i in range(peers) if 0 <= i + by < peers]
    return lax.ppermute(x, axis, pairs)


def element_rows(nodes):
    triples = nodes.T[:, :, None] * 3 + jnp.arange(3, dtype=jnp.int32)[None, None, :]
    flattened = triples.reshape(nodes.shape[1], -1)
    padding = jnp.zeros((nodes.shape[1], EDOF - flattened.shape[1]), jnp.int32)
    return jnp.concatenate([flattened, padding], axis=1)


def project(left_rows, right_rows):
    return jnp.einsum("rc,rd->cd", left_rows, right_rows, preferred_element_type=jnp.float32)


FINE = ("zh", "c", "x", "zl", "y")
FINE_SIZES = (4, 2, 4, 4, 4)


def group_sum(chunk, axis):
    size = lax.axis_size(axis)
    return lax.all_to_all(chunk.reshape(size, -1), axis, 0, 0, tiled=False).sum(0)


def group_gather(chunk, axis):
    size = lax.axis_size(axis)
    copies = jnp.broadcast_to(chunk[None], (size,) + chunk.shape)
    return lax.all_to_all(copies, axis, 0, 0, tiled=False).reshape(-1)


def summed_everywhere(flat, axes):
    if axes != FINE or flat.shape[0] % 512:
        return lax.psum(flat, axes)
    count = 512
    me = lax.axis_index(axes)
    core_pairs = [(i, i ^ 64) for i in range(count)]
    upper = (me >> 6) & 1
    half = flat.shape[0] // 2
    low, high = flat[:half], flat[half:]
    keep = jnp.where(upper == 0, low, high)
    send = jnp.where(upper == 0, high, low)
    current = keep + lax.ppermute(send, axes, core_pairs)
    for group in (("zl", "y"), ("zh", "x")):
        current = group_sum(current, group)
    for group in (("zh", "x"), ("zl", "y")):
        current = group_gather(current, group)
    other = lax.ppermute(current, axes, core_pairs)
    return jnp.where(
        upper == 0,
        jnp.concatenate([current, other]),
        jnp.concatenate([other, current]),
    )


def local(axes, reduced_basis, tangents, connectivity, weights):
    own_rows, columns = reduced_basis.shape
    rim_rows = RIM * 3
    rim_basis = passed_along(reduced_basis[:rim_rows], axes, -1)
    extended = jnp.concatenate([reduced_basis, rim_basis], axis=0)

    assembled = element_stage(extended, tangents, connectivity, weights)
    incoming = passed_along(assembled[own_rows:], axes, 1)
    residual_rows = assembled[:own_rows].at[:rim_rows].add(incoming).astype(jnp.bfloat16)
    galerkin_part = project(reduced_basis, residual_rows)
    lspg_part = project(residual_rows, residual_rows)
    both = jnp.stack([galerkin_part, lspg_part]).reshape(-1)
    galerkin_sum, lspg_sum = summed_everywhere(both, axes).reshape(2, columns, columns)
    total_dofs = own_rows * lax.axis_size(axes)
    scale_factor = 1.0 / float(total_dofs)
    return (residual_rows, galerkin_sum * scale_factor, lspg_sum * scale_factor)


def solution(mesh):
    axes = AXES
    if tuple(mesh.devices.shape) == (8, 64):
        mesh = Mesh(mesh.devices.reshape(FINE_SIZES), FINE)
        axes = FINE
    placed = (
        P(axes, None),
        P(axes, None),
        P(None, axes),
        P(axes),
    )
    return jax.shard_map(
        functools.partial(local, axes),
        mesh=mesh,
        in_specs=placed,
        out_specs=(P(axes, None), P(), P()),
        check_vma=False,
    )
```

```python
import functools

import jax
import jax.numpy as jnp
from jax import lax
from jax.experimental import pallas as pl
from jax.experimental.pallas import tpu as pltpu
from jax.sharding import Mesh, PartitionSpec as P

EDOF = 64
RIM = 128
AXES = ("grp", "dom")
WIN = 208


def window_tables(connectivity, ext_rows):
    npe, elems = connectivity.shape
    ext_nodes = ext_rows // 3
    nodes = connectivity.T
    index = jnp.arange(elems, dtype=jnp.int32)[:, None]
    outlier = ((index == 0) & (nodes == 0)) | ((index == elems - 1) & (nodes == ext_nodes - 1))
    low = jnp.min(jnp.where(outlier, ext_nodes, nodes), axis=1)
    low = jnp.where(low == ext_nodes, 0, low)
    first = jnp.clip((3 * low) // 16 * 16, 0, ext_rows - WIN)
    second = jnp.where(index[:, 0] == elems - 1, ext_rows - WIN, 0)
    rows = (nodes[:, :, None] * 3 + jnp.arange(3, dtype=jnp.int32)).reshape(elems, -1)
    pad = jnp.full((elems, EDOF - rows.shape[1]), -1, jnp.int32)
    slot_out = jnp.repeat(outlier, 3, axis=1)
    off1 = jnp.concatenate([jnp.where(slot_out, -1, rows - first[:, None]), pad], axis=1)
    off2 = jnp.concatenate([jnp.where(slot_out, rows - second[:, None], -1), pad], axis=1)
    return first.astype(jnp.int32), second.astype(jnp.int32), off1, off2


def element_kernel(first_ref, second_ref, w_ref, basis_ref, rim_ref, k_ref, r1_ref, r2_ref, acc_ref, x_ref):
    elems = k_ref.shape[0]
    own = basis_ref.shape[0]
    x_ref[pl.ds(0, own), :] = basis_ref[...]
    x_ref[pl.ds(own, rim_ref.shape[0]), :] = rim_ref[...]
    acc_ref[...] = jnp.zeros_like(acc_ref)
    row_iota = lax.broadcasted_iota(jnp.int32, (WIN, EDOF), 0)
    eye = (
        lax.broadcasted_iota(jnp.int32, (EDOF, EDOF), 0)
        == lax.broadcasted_iota(jnp.int32, (EDOF, EDOF), 1)
    ).astype(jnp.bfloat16)
    both = ((first_ref, r1_ref), (second_ref, r2_ref))

    def one(e, windows):
        gathered = None
        picks = []
        for start_ref, row_ref in windows:
            start = pl.multiple_of(start_ref[e], 16)
            spread = (row_ref[pl.ds(e, 1), :] == row_iota).astype(jnp.bfloat16)
            pick = lax.dot_general(
                eye, spread, (((1,), (1,)), ((), ())), preferred_element_type=jnp.float32
            ).astype(jnp.bfloat16)
            part = jnp.dot(pick, x_ref[pl.ds(start, WIN), :], preferred_element_type=jnp.float32)
            gathered = part if gathered is None else gathered + part
            picks.append((start, spread))
        products = jnp.dot(k_ref[e], gathered.astype(jnp.bfloat16), preferred_element_type=jnp.float32)
        scaled = products * w_ref[e]
        high = scaled.astype(jnp.bfloat16)
        rest = scaled - high.astype(jnp.float32)
        mid = rest.astype(jnp.bfloat16)
        parts = jnp.concatenate([high, mid], axis=1)
        cols = scaled.shape[1]
        for start, spread in picks:
            moved = jnp.dot(spread, parts, preferred_element_type=jnp.float32)
            total = moved[:, :cols] + moved[:, cols:]
            acc_ref[pl.ds(start, WIN), :] += total

    one(0, both)

    def body(e, carry):
        one(e, both[:1])
        return carry

    lax.fori_loop(1, elems - 1, body, 0, unroll=16)
    one(elems - 1, both)


def element_stage(basis, rim, tangents, connectivity, weights):
    own_rows, cols = basis.shape
    ext_rows = own_rows + rim.shape[0]
    elems = weights.shape[0]
    first, second, off1, off2 = window_tables(connectivity, ext_rows)
    k = tangents.reshape(elems, EDOF, EDOF)
    return pl.pallas_call(
        element_kernel,
        out_shape=jax.ShapeDtypeStruct((ext_rows, cols), jnp.float32),
        in_specs=[pl.BlockSpec(memory_space=pltpu.SMEM)] * 3
        + [pl.BlockSpec(memory_space=pltpu.VMEM)] * 5,
        out_specs=pl.BlockSpec(memory_space=pltpu.VMEM),
        scratch_shapes=[pltpu.VMEM((ext_rows, cols), basis.dtype)],
        compiler_params=pltpu.CompilerParams(vmem_limit_bytes=48 * 1024 * 1024),
    )(first, second, weights, basis, rim, k, off1, off2)


def passed_along(x, axis, by):
    peers = lax.axis_size(axis)
    pairs = [(i, i + by) for i in range(peers) if 0 <= i + by < peers]
    return lax.ppermute(x, axis, pairs)


def element_rows(nodes):
    triples = nodes.T[:, :, None] * 3 + jnp.arange(3, dtype=jnp.int32)[None, None, :]
    flattened = triples.reshape(nodes.shape[1], -1)
    padding = jnp.zeros((nodes.shape[1], EDOF - flattened.shape[1]), jnp.int32)
    return jnp.concatenate([flattened, padding], axis=1)


def project(left_rows, right_rows):
    return jnp.einsum("rc,rd->cd", left_rows, right_rows, preferred_element_type=jnp.float32)


FINE = ("zh", "c", "x", "zl", "y")
FINE_SIZES = (4, 2, 4, 4, 4)


def group_sum(chunk, axis):
    size = lax.axis_size(axis)
    return lax.all_to_all(chunk.reshape(size, -1), axis, 0, 0, tiled=False).sum(0)


def group_gather(chunk, axis):
    size = lax.axis_size(axis)
    copies = jnp.broadcast_to(chunk[None], (size,) + chunk.shape)
    return lax.all_to_all(copies, axis, 0, 0, tiled=False).reshape(-1)


def summed_everywhere(flat, axes):
    if axes != FINE or flat.shape[0] % 512:
        return lax.psum(flat, axes)
    count = 512
    me = lax.axis_index(axes)
    core_pairs = [(i, i ^ 64) for i in range(count)]
    upper = (me >> 6) & 1
    half = flat.shape[0] // 2
    low, high = flat[:half], flat[half:]
    keep = jnp.where(upper == 0, low, high)
    send = jnp.where(upper == 0, high, low)
    current = keep + lax.ppermute(send, axes, core_pairs)
    for group in (("zl", "y"), ("zh", "x")):
        current = group_sum(current, group)
    for group in (("zh", "x"), ("zl", "y")):
        current = group_gather(current, group)
    other = lax.ppermute(current, axes, core_pairs)
    return jnp.where(
        upper == 0,
        jnp.concatenate([current, other]),
        jnp.concatenate([other, current]),
    )


def local(axes, reduced_basis, tangents, connectivity, weights):
    own_rows, columns = reduced_basis.shape
    rim_rows = RIM * 3
    rim_basis = passed_along(reduced_basis[:rim_rows], axes, -1)

    assembled = element_stage(reduced_basis, rim_basis, tangents, connectivity, weights)
    incoming = passed_along(assembled[own_rows:], axes, 1)
    residual_rows = assembled[:own_rows].at[:rim_rows].add(incoming).astype(jnp.bfloat16)
    galerkin_part = project(reduced_basis, residual_rows)
    lspg_part = project(residual_rows, residual_rows)
    both = jnp.stack([galerkin_part, lspg_part]).reshape(-1)
    galerkin_sum, lspg_sum = summed_everywhere(both, axes).reshape(2, columns, columns)
    total_dofs = own_rows * lax.axis_size(axes)
    scale_factor = 1.0 / float(total_dofs)
    return (residual_rows, galerkin_sum * scale_factor, lspg_sum * scale_factor)


def solution(mesh):
    axes = AXES
    if tuple(mesh.devices.shape) == (8, 64):
        mesh = Mesh(mesh.devices.reshape(FINE_SIZES), FINE)
        axes = FINE
    placed = (
        P(axes, None),
        P(axes, None),
        P(None, axes),
        P(axes),
    )
    return jax.shard_map(
        functools.partial(local, axes),
        mesh=mesh,
        in_specs=placed,
        out_specs=(P(axes, None), P(), P()),
        check_vma=False,
    )
```
